1024 devices in a mesh: ctx: 64 (over y, z), tp: 16 (over x, core).
Axes of the slice: x: 8, y: 8, z: 8, core: 2. Of those that a mesh axis runs over, the one named last changes fastest.
Arguments:
- x_in: bfloat16 [4096, 8192], P('ctx', 'tp'), may hold values from -6 to 6
- z_in: bfloat16 [4096, 8192], P('ctx', 'tp'), may hold values from -6 to 6
- b_in: bfloat16 [4096, 4, 256], P('ctx'), may hold values from -6 to 6
- c_in: bfloat16 [4096, 4, 256], P('ctx'), may hold values from -6 to 6
- conv_x: bfloat16 [4, 8192], P(None, 'tp'), may hold values from -3 to 3
- conv_bc: bfloat16 [4, 2, 4, 256], replicated, may hold values from -3 to 3
- dt_raw: float32 [4096, 128], P('ctx', 'tp'), may hold values from -5 to 5
- dt_bias: float32 [128], P('tp'), may hold values from -1 to 1
- decay_rate: float32 [128], P('tp'), may hold values from 1.2207031e-05 to 0.05
- d_skip: float32 [128], P('tp'), may hold values from 0.5 to 1.5
- norm_gain: float32 [8192], P('tp'), may hold values from 0.1 to 1.9
- w_out: bfloat16 [8192, 8192], P('tp'), may hold values from -0.0625 to 0.0625
Outputs:
- mixed: bfloat16 [4096, 8192], P('ctx', 'tp')
The draws below stay inside these ranges and needn't reach their ends.
All inputs are finite; a program needn't handle non-finite values.
Results may differ from the reference program's by a relative error of at most 0.022.
Values may be sent and summed in bfloat16 or wider, within the bound.
No kernel may reach another device: no remote copies, remote signals or barrier semaphores. Data moves between devices by JAX's collectives and lax.ppermute only.
A program may use at most 128 MiB of HBM per device.

```python
import math
import jax
import jax.numpy as jnp
from jax import lax

D = 8192
HEADS = 128
HEAD_DIM = 64
STATE = 256
GROUPS = 4
CONV = 4
TOK_DEV = 64
TOKENS = 4096
INNER = 8192
N_CTX = 64
N_TP = 16


def level_of(rng, extent, pieces, least, top_value):
    gain = 1.0
    for dim, blocks in pieces:
        draws = jax.random.uniform(jax.random.fold_in(jax.random.fold_in(rng, 6), dim), (blocks,), jnp.float32, least / len(pieces), top_value / len(pieces))
        gain = gain * jnp.repeat(jnp.exp(draws), extent[dim] // blocks).reshape((-1,) + (1,) * (len(extent) - 1 - dim))
    return gain


def gaussian(own_key, extent, deviation, reach, cuts=(), kind=jnp.bfloat16):
    factor_of = level_of(own_key, extent, cuts, -0.22, 0.18) if cuts else 1.0
    entries = jax.random.normal(own_key, extent, jnp.float32) * deviation * factor_of
    return jnp.minimum(jnp.maximum(entries, -reach), reach).astype(kind)


def setup_inputs(seed: int = 0) -> dict:
    key_of = jax.random.split(jax.random.key(seed), 13)
    x_in = gaussian(key_of[0], (TOKENS, INNER), 1.0, 6.0, ((0, 64), (1, 16)))
    z_in = gaussian(key_of[1], (TOKENS, INNER), 1.0, 6.0, ((0, 64), (1, 16)))
    b_in = gaussian(key_of[2], (TOKENS, GROUPS, STATE), 1.0, 6.0, ((0, 64),))
    c_in = gaussian(key_of[3], (TOKENS, GROUPS, STATE), 1.0, 6.0, ((0, 64),))
    conv_x = gaussian(key_of[4], (CONV, INNER), CONV ** -0.5, 3.0, ((1, 16),))
    conv_bc = gaussian(key_of[5], (CONV, 2, GROUPS, STATE), CONV ** -0.5, 3.0)
    dt_raw = gaussian(key_of[6], (TOKENS, HEADS), 1.0, 5.0, ((0, 64), (1, 16)), jnp.float32)
    dt_bias = jnp.clip(jax.random.uniform(key_of[7], (HEADS,), jnp.float32, -1.0, 1.0) * level_of(key_of[7], (HEADS,), ((0, 16),), -0.4, 0.0), -1.0, 1.0)
    decay_rate = jnp.clip(jnp.exp(math.log(0.05) - 8.317766 * jax.random.uniform(key_of[8], (HEADS,), jnp.float32) ** level_of(key_of[8], (HEADS,), ((0, 16),), -0.2, 0.2)), 1.220703143189894e-05, 0.05)
    d_skip = jnp.clip(0.5 + 1.0 * jax.random.uniform(key_of[9], (HEADS,), jnp.float32) ** level_of(key_of[9], (HEADS,), ((0, 16),), -0.2, 0.2), 0.5, 1.5)
    norm_gain = jnp.clip(1.0 + 0.18 * jax.random.normal(key_of[10], (INNER,), jnp.float32), 0.1, 1.9)
    w_out = gaussian(key_of[11], (INNER, D), INNER ** -0.5, 0.0625, ((0, 16),))
    return {"x_in": x_in, "z_in": z_in, "b_in": b_in, "c_in": c_in, "conv_x": conv_x, "conv_bc": conv_bc, "dt_raw": dt_raw, "dt_bias": dt_bias, "decay_rate": decay_rate, "d_skip": d_skip, "norm_gain": norm_gain, "w_out": w_out}


def causal_conv(sequence, taps):
    width = taps.shape[0]
    length = sequence.shape[0]
    padded = jnp.concatenate([jnp.zeros((width - 1, sequence.shape[1]), sequence.dtype), sequence], 0).astype(jnp.float32)
    kernel = taps.astype(jnp.float32)
    total = jnp.zeros((length, sequence.shape[1]), jnp.float32)
    for offset in range(width):
        total = total + padded[offset:offset + length] * kernel[offset]
    return jax.nn.silu(total).astype(jnp.bfloat16)

def block_step(state, inputs):
    xconv, bconv, cconv, delta, decay_rate, d_skip = inputs
    repeat = HEADS // GROUPS
    rate = -decay_rate[None, :] * delta
    cumulative = jnp.cumsum(rate, axis=0)
    along = cumulative.T
    length = xconv.shape[0]
    causal = (jnp.arange(length)[:, None] >= jnp.arange(length)[None, :])[None]
    spread = along[:, :, None] - along[:, None, :]
    factor = jnp.where(causal, jnp.exp(jnp.where(causal, spread, 0.0)), 0.0) * delta.T[:, None, :]
    intersection = jnp.einsum('tgn,sgn->gts', cconv.astype(jnp.float32), bconv.astype(jnp.float32))
    intersection = jnp.repeat(intersection, repeat, axis=0)
    mixing = (intersection * factor).astype(jnp.bfloat16)
    inner_out = jnp.einsum('hts,shp->thp', mixing.astype(jnp.float32), xconv.astype(jnp.float32))
    tail_weight = jnp.exp(cumulative[-1][None, :] - cumulative) * delta
    weighted = (tail_weight[:, :, None] * xconv.astype(jnp.float32)).astype(jnp.bfloat16)
    keys_head = jnp.repeat(bconv, repeat, axis=1)
    local_state = jnp.einsum('shp,shn->hpn', weighted.astype(jnp.float32), keys_head.astype(jnp.float32))
    queries = jnp.repeat(cconv, repeat, axis=1).astype(jnp.float32)
    carried = jnp.einsum('thn,hpn->thp', queries, state, precision=lax.Precision.HIGHEST) * jnp.exp(cumulative)[:, :, None]
    ssm_out = inner_out + carried + d_skip[None, :, None] * xconv.astype(jnp.float32)
    new_state = jnp.exp(cumulative[-1])[:, None, None] * state + local_state
    return (new_state, ssm_out)

def reference(x_in, z_in, b_in, c_in, conv_x, conv_bc, dt_raw, dt_bias, decay_rate, d_skip, norm_gain, w_out):
    xconv = causal_conv(x_in, conv_x).reshape(N_CTX, TOK_DEV, HEADS, HEAD_DIM)
    joined = jnp.concatenate([b_in.reshape(TOKENS, GROUPS * STATE), c_in.reshape(TOKENS, GROUPS * STATE)], 1)
    joined_conv = causal_conv(joined, conv_bc.reshape(CONV, 2 * GROUPS * STATE))
    bconv = joined_conv[:, :GROUPS * STATE].reshape(N_CTX, TOK_DEV, GROUPS, STATE)
    cconv = joined_conv[:, GROUPS * STATE:].reshape(N_CTX, TOK_DEV, GROUPS, STATE)
    delta = jax.nn.softplus(dt_raw + dt_bias[None, :]).reshape(N_CTX, TOK_DEV, HEADS)

    def step(state, inputs):
        return block_step(state, (inputs[0], inputs[1], inputs[2], inputs[3], decay_rate, d_skip))
    start = jnp.zeros((HEADS, HEAD_DIM, STATE), jnp.float32)
    final, outputs = lax.scan(step, start, (xconv, bconv, cconv, delta))
    gated = outputs.reshape(TOKENS, INNER) * jax.nn.silu(z_in.astype(jnp.float32))
    norm_size = HEADS // GROUPS * HEAD_DIM
    grouped = gated.reshape(TOKENS, GROUPS, norm_size)
    squares = lax.optimization_barrier(jnp.sum(grouped * grouped, axis=-1))
    scale = lax.rsqrt(squares / norm_size + 1e-05)
    hidden = ((grouped * scale[:, :, None]).reshape(TOKENS, INNER) * norm_gain[None, :]).astype(jnp.bfloat16)
    block_rows = INNER // N_TP
    hidden_blocks = hidden.reshape(TOKENS, N_TP, block_rows).transpose(1, 0, 2)
    weight_blocks = w_out.reshape(N_TP, block_rows, D)

    def project(total, block):
        part = jnp.dot(block[0], block[1], preferred_element_type=jnp.float32)
        rounded = lax.optimization_barrier(part.astype(jnp.bfloat16))
        return (total + rounded.astype(jnp.float32), None)
    summed, unused = lax.scan(project, jnp.zeros((TOKENS, D), jnp.float32), (hidden_blocks, weight_blocks))
    return summed.astype(jnp.bfloat16)
```

```python
import jax
import jax.numpy as jnp
from jax import lax
from jax.sharding import PartitionSpec as P

HEADS = 128
HEAD_DIM = 64
STATE = 256
GROUPS = 4
CONV = 4
SIDE = 128


def shifted(block, axis, distance):
    devices = range(lax.axis_size(axis))
    route = [(i - distance, i) for i in devices if i - distance in devices]
    return lax.ppermute(block, axis, route)


def group_sum(value, axis, span):
    total = value
    step = 1
    while step < span:
        route = [(i, i ^ step) for i in range(lax.axis_size(axis))]
        total = total + lax.ppermute(total, axis, route)
        step *= 2
    return total


def causal_conv(tail, sequence, taps):
    length = sequence.shape[0]
    padded = jnp.concatenate([tail, sequence], 0).astype(jnp.float32)
    kernel = taps.astype(jnp.float32)
    total = jnp.zeros(sequence.shape, jnp.float32)
    for offset in range(taps.shape[0]):
        total = total + padded[offset : offset + length] * kernel[offset]
    return jax.nn.silu(total).astype(jnp.bfloat16)


def split3(value):
    hi = value.astype(jnp.bfloat16)
    rest = value - hi.astype(jnp.float32)
    mid = rest.astype(jnp.bfloat16)
    lo = (rest - mid.astype(jnp.float32)).astype(jnp.bfloat16)
    return hi, mid, lo


def local(
    x_in, z_in, b_in, c_in, conv_x, conv_bc, dt_raw, dt_bias, decay_rate, d_skip, norm_gain, w_out
):
    length, channels = x_in.shape
    heads_here = dt_raw.shape[1]
    per_group = HEADS // GROUPS
    local_groups = max(heads_here // per_group, 1)
    repeat = heads_here // local_groups
    first_group = lax.axis_index("tp") * heads_here // per_group
    b_here = lax.dynamic_slice_in_dim(b_in, first_group, local_groups, 1).reshape(
        length, local_groups * STATE
    )
    c_here = lax.dynamic_slice_in_dim(c_in, first_group, local_groups, 1).reshape(
        length, local_groups * STATE
    )
    taps_here = lax.dynamic_slice_in_dim(conv_bc, first_group, local_groups, 2).reshape(
        CONV, 2 * local_groups * STATE
    )
    joined = jnp.concatenate([b_here, c_here], 1)
    x_tail, joined_tail = shifted(
        (x_in[length - CONV + 1 :], joined[length - CONV + 1 :]), "ctx", 1
    )
    xconv = causal_conv(x_tail, x_in, conv_x).reshape(length, heads_here, HEAD_DIM)
    joined_conv = causal_conv(joined_tail, joined, taps_here)
    bconv = joined_conv[:, : local_groups * STATE].reshape(length, local_groups, STATE)
    cconv = joined_conv[:, local_groups * STATE :].reshape(length, local_groups, STATE)
    delta = jax.nn.softplus(dt_raw + dt_bias[None, :])
    rate = -decay_rate[None, :] * delta
    cumulative = jnp.cumsum(rate, axis=0)
    along = cumulative.T
    causal = (jnp.arange(length)[:, None] >= jnp.arange(length)[None, :])[None]
    spread = along[:, :, None] - along[:, None, :]
    factor = jnp.where(causal, jnp.exp(jnp.where(causal, spread, 0.0)), 0.0) * delta.T[:, None, :]
    intersection = jnp.einsum("tgn,sgn->gts", cconv, bconv, preferred_element_type=jnp.float32)
    intersection = jnp.repeat(intersection, repeat, axis=0)
    mixing = (intersection * factor).astype(jnp.bfloat16)
    inner_out = jnp.einsum("hts,shp->thp", mixing, xconv, preferred_element_type=jnp.float32)
    tail_weight = jnp.exp(cumulative[-1][None, :] - cumulative) * delta
    weighted = (tail_weight[:, :, None] * xconv.astype(jnp.float32)).astype(jnp.bfloat16)

    cum_last = cumulative[-1]
    side = jnp.zeros((length, SIDE), jnp.bfloat16)
    side = side.at[0:3, 0:heads_here].set(jnp.stack(split3(cum_last)))
    packet = jnp.concatenate(
        [weighted.reshape(length, channels), bconv.reshape(length, local_groups * STATE), side], 1
    )
    gathered = lax.all_gather(packet, "ctx")
    blocks = gathered.shape[0]
    mine = lax.axis_index("ctx")
    w_all = gathered[:, :, :channels]
    b_all = gathered[:, :, channels : channels + local_groups * STATE]
    pieces = gathered[:, 0:3, channels + local_groups * STATE :][:, :, :heads_here].astype(
        jnp.float32
    )
    lasts = pieces[:, 0] + pieces[:, 1] + pieces[:, 2]
    order = jnp.arange(blocks)
    between = (order[:, None] < order[None, :]) & (order[None, :] < mine)
    span = jnp.sum(jnp.where(between[:, :, None], lasts[None, :, :], 0.0), axis=1)
    gain = jnp.where((order < mine)[:, None], jnp.exp(span), 0.0)
    gain = gain.reshape(blocks, 1, local_groups, repeat, 1)
    w_scaled = (
        w_all.reshape(blocks, length, local_groups, repeat, HEAD_DIM).astype(jnp.float32) * gain
    )
    b_all = b_all.reshape(blocks, length, local_groups, STATE)
    scores = jnp.einsum("tgn,jsgn->gtjs", cconv, b_all, preferred_element_type=jnp.float32)
    carried = jnp.einsum(
        "gtjs,jsgrp->tgrp", scores, w_scaled, precision=lax.Precision.HIGHEST,
        preferred_element_type=jnp.float32,
    ).reshape(length, heads_here, HEAD_DIM)
    carried = carried * jnp.exp(cumulative)[:, :, None]
    ssm_out = inner_out + carried + d_skip[None, :, None] * xconv.astype(jnp.float32)
    gated = ssm_out.reshape(length, channels) * jax.nn.silu(z_in.astype(jnp.float32))
    norm_size = per_group * HEAD_DIM
    grouped = gated.reshape(length, local_groups, channels // local_groups)
    partial_squares = jnp.sum(grouped * grouped, axis=-1)
    if local_groups == 1:
        squares = group_sum(partial_squares, "tp", per_group // heads_here)
    else:
        squares = partial_squares
    scale = lax.rsqrt(squares / norm_size + 1e-05)
    hidden = ((grouped * scale[:, :, None]).reshape(length, channels) * norm_gain[None, :]).astype(
        jnp.bfloat16
    )
    partial_out = jnp.dot(hidden, w_out, preferred_element_type=jnp.float32)
    summed = lax.psum_scatter(
        partial_out.astype(jnp.bfloat16), "tp", scatter_dimension=1, tiled=True
    )
    return summed


def solution(mesh):
    return jax.shard_map(
        local,
        mesh=mesh,
        in_specs=(
            P("ctx", "tp"),
            P("ctx", "tp"),
            P("ctx", None, None),
            P("ctx", None, None),
            P(None, "tp"),
            P(),
            P("ctx", "tp"),
            P("tp"),
            P("tp"),
            P("tp"),
            P("tp"),
            P("tp", None),
        ),
        out_specs=P("ctx", "tp"),
        check_vma=False,
    )
```

```python
import jax
import jax.numpy as jnp
from jax import lax
from jax.sharding import PartitionSpec as P

HEADS = 128
HEAD_DIM = 64
STATE = 256
GROUPS = 4
CONV = 4
SIDE = 128


def shifted(block, axis, distance):
    devices = range(lax.axis_size(axis))
    route = [(i - distance, i) for i in devices if i - distance in devices]
    return lax.ppermute(block, axis, route)


def group_sum(value, axis, span):
    total = value
    step = 1
    while step < span:
        route = [(i, i ^ step) for i in range(lax.axis_size(axis))]
        total = total + lax.ppermute(total, axis, route)
        step *= 2
    return total


def causal_conv(tail, sequence, taps):
    length = sequence.shape[0]
    padded = jnp.concatenate([tail, sequence], 0).astype(jnp.float32)
    kernel = taps.astype(jnp.float32)
    total = jnp.zeros(sequence.shape, jnp.float32)
    for offset in range(taps.shape[0]):
        total = total + padded[offset : offset + length] * kernel[offset]
    return jax.nn.silu(total).astype(jnp.bfloat16)


def split3(value):
    hi = value.astype(jnp.bfloat16)
    rest = value - hi.astype(jnp.float32)
    mid = rest.astype(jnp.bfloat16)
    lo = (rest - mid.astype(jnp.float32)).astype(jnp.bfloat16)
    return hi, mid, lo


def local(
    x_in, z_in, b_in, c_in, conv_x, conv_bc, dt_raw, dt_bias, decay_rate, d_skip, norm_gain, w_out
):
    length, channels = x_in.shape
    heads_here = dt_raw.shape[1]
    per_group = HEADS // GROUPS
    local_groups = max(heads_here // per_group, 1)
    repeat = heads_here // local_groups
    first_group = lax.axis_index("tp") * heads_here // per_group
    b_here = lax.dynamic_slice_in_dim(b_in, first_group, local_groups, 1).reshape(
        length, local_groups * STATE
    )
    c_here = lax.dynamic_slice_in_dim(c_in, first_group, local_groups, 1).reshape(
        length, local_groups * STATE
    )
    taps_here = lax.dynamic_slice_in_dim(conv_bc, first_group, local_groups, 2).reshape(
        CONV, 2 * local_groups * STATE
    )
    joined = jnp.concatenate([b_here, c_here], 1)
    x_tail, joined_tail = shifted(
        (x_in[length - CONV + 1 :], joined[length - CONV + 1 :]), "ctx", 1
    )
    xconv = causal_conv(x_tail, x_in, conv_x).reshape(length, heads_here, HEAD_DIM)
    joined_conv = causal_conv(joined_tail, joined, taps_here)
    bconv = joined_conv[:, : local_groups * STATE].reshape(length, local_groups, STATE)
    cconv = joined_conv[:, local_groups * STATE :].reshape(length, local_groups, STATE)
    delta = jax.nn.softplus(dt_raw + dt_bias[None, :])
    rate = -decay_rate[None, :] * delta
    cumulative = jnp.cumsum(rate, axis=0)
    along = cumulative.T
    causal = (jnp.arange(length)[:, None] >= jnp.arange(length)[None, :])[None]
    spread = along[:, :, None] - along[:, None, :]
    factor = jnp.where(causal, jnp.exp(jnp.where(causal, spread, 0.0)), 0.0) * delta.T[:, None, :]
    intersection = jnp.einsum("tgn,sgn->gts", cconv, bconv, preferred_element_type=jnp.float32)
    intersection = jnp.repeat(intersection, repeat, axis=0)
    mixing = (intersection * factor).astype(jnp.bfloat16)
    inner_out = jnp.einsum("hts,shp->thp", mixing, xconv, preferred_element_type=jnp.float32)
    tail_weight = jnp.exp(cumulative[-1][None, :] - cumulative) * delta
    weighted = (tail_weight[:, :, None] * xconv.astype(jnp.float32)).astype(jnp.bfloat16)

    cum_last = cumulative[-1]
    side = jnp.zeros((length, SIDE), jnp.bfloat16)
    side = side.at[0:3, 0:heads_here].set(jnp.stack(split3(cum_last)))
    packet = jnp.concatenate(
        [weighted.reshape(length, channels), bconv.reshape(length, local_groups * STATE), side], 1
    )
    gathered = lax.all_gather(packet, "ctx")
    blocks = gathered.shape[0]
    mine = lax.axis_index("ctx")
    w_all = gathered[:, :, :channels]
    b_all = gathered[:, :, channels : channels + local_groups * STATE]
    pieces = gathered[:, 0:3, channels + local_groups * STATE :][:, :, :heads_here].astype(
        jnp.float32
    )
    lasts = pieces[:, 0] + pieces[:, 1] + pieces[:, 2]
    order = jnp.arange(blocks)
    between = (order[:, None] < order[None, :]) & (order[None, :] < mine)
    span = jnp.sum(jnp.where(between[:, :, None], lasts[None, :, :], 0.0), axis=1)
    gain = jnp.where((order < mine)[:, None], jnp.exp(span), 0.0)
    gain = jnp.repeat(gain, HEAD_DIM, axis=1)[:, None, :]
    w_scaled = (w_all.astype(jnp.float32) * gain).reshape(blocks * length, channels)
    w_hi = w_scaled.astype(jnp.bfloat16)
    w_lo = (w_scaled - w_hi.astype(jnp.float32)).astype(jnp.bfloat16)
    b_flat = b_all.reshape(blocks * length, local_groups * STATE)
    c_flat = cconv.reshape(length, local_groups * STATE)
    scores = lax.dot_general(
        c_flat, b_flat, (((1,), (1,)), ((), ())), preferred_element_type=jnp.float32
    )
    s_hi = scores.astype(jnp.bfloat16)
    s_lo = (scores - s_hi.astype(jnp.float32)).astype(jnp.bfloat16)
    carried = (
        jnp.dot(s_hi, w_hi, preferred_element_type=jnp.float32)
        + jnp.dot(s_lo, w_hi, preferred_element_type=jnp.float32)
        + jnp.dot(s_hi, w_lo, preferred_element_type=jnp.float32)
    ).reshape(length, heads_here, HEAD_DIM)
    carried = carried * jnp.exp(cumulative)[:, :, None]
    ssm_out = inner_out + carried + d_skip[None, :, None] * xconv.astype(jnp.float32)
    gated = ssm_out.reshape(length, channels) * jax.nn.silu(z_in.astype(jnp.float32))
    norm_size = per_group * HEAD_DIM
    grouped = gated.reshape(length, local_groups, channels // local_groups)
    partial_squares = jnp.sum(grouped * grouped, axis=-1)
    if local_groups == 1:
        squares = group_sum(partial_squares, "tp", per_group // heads_here)
    else:
        squares = partial_squares
    scale = lax.rsqrt(squares / norm_size + 1e-05)
    hidden = ((grouped * scale[:, :, None]).reshape(length, channels) * norm_gain[None, :]).astype(
        jnp.bfloat16
    )
    partial_out = jnp.dot(hidden, w_out, preferred_element_type=jnp.float32)
    summed = lax.psum_scatter(
        partial_out.astype(jnp.bfloat16), "tp", scatter_dimension=1, tiled=True
    )
    return summed


def solution(mesh):
    return jax.shard_map(
        local,
        mesh=mesh,
        in_specs=(
            P("ctx", "tp"),
            P("ctx", "tp"),
            P("ctx", None, None),
            P("ctx", None, None),
            P(None, "tp"),
            P(),
            P("ctx", "tp"),
            P("tp"),
            P("tp"),
            P("tp"),
            P("tp"),
            P("tp", None),
        ),
        out_specs=P("ctx", "tp"),
        check_vma=False,
    )
```

```python
import jax
import jax.numpy as jnp
from jax import lax
from jax.sharding import PartitionSpec as P

HEADS = 128
HEAD_DIM = 64
STATE = 256
GROUPS = 4
CONV = 4
SIDE = 128


def shifted(block, axis, distance):
    devices = range(lax.axis_size(axis))
    route = [(i - distance, i) for i in devices if i - distance in devices]
    return lax.ppermute(block, axis, route)


def group_sum(value, axis, span):
    total = value
    step = 1
    while step < span:
        route = [(i, i ^ step) for i in range(lax.axis_size(axis))]
        total = total + lax.ppermute(total, axis, route)
        step *= 2
    return total


def causal_conv(tail, sequence, taps):
    length = sequence.shape[0]
    padded = jnp.concatenate([tail, sequence], 0).astype(jnp.float32)
    kernel = taps.astype(jnp.float32)
    total = jnp.zeros(sequence.shape, jnp.float32)
    for offset in range(taps.shape[0]):
        total = total + padded[offset : offset + length] * kernel[offset]
    return jax.nn.silu(total).astype(jnp.bfloat16)


def split3(value):
    hi = value.astype(jnp.bfloat16)
    rest = value - hi.astype(jnp.float32)
    mid = rest.astype(jnp.bfloat16)
    lo = (rest - mid.astype(jnp.float32)).astype(jnp.bfloat16)
    return hi, mid, lo


def local(
    x_in, z_in, b_in, c_in, conv_x, conv_bc, dt_raw, dt_bias, decay_rate, d_skip, norm_gain, w_out
):
    length, channels = x_in.shape
    heads_here = dt_raw.shape[1]
    per_group = HEADS // GROUPS
    local_groups = max(heads_here // per_group, 1)
    repeat = heads_here // local_groups
    first_group = lax.axis_index("tp") * heads_here // per_group
    b_here = lax.dynamic_slice_in_dim(b_in, first_group, local_groups, 1).reshape(
        length, local_groups * STATE
    )
    c_here = lax.dynamic_slice_in_dim(c_in, first_group, local_groups, 1).reshape(
        length, local_groups * STATE
    )
    taps_here = lax.dynamic_slice_in_dim(conv_bc, first_group, local_groups, 2).reshape(
        CONV, 2 * local_groups * STATE
    )
    joined = jnp.concatenate([b_here, c_here], 1)
    x_tail, joined_tail = shifted(
        (x_in[length - CONV + 1 :], joined[length - CONV + 1 :]), "ctx", 1
    )
    xconv = causal_conv(x_tail, x_in, conv_x).reshape(length, heads_here, HEAD_DIM)
    joined_conv = causal_conv(joined_tail, joined, taps_here)
    bconv = joined_conv[:, : local_groups * STATE].reshape(length, local_groups, STATE)
    cconv = joined_conv[:, local_groups * STATE :].reshape(length, local_groups, STATE)
    delta = jax.nn.softplus(dt_raw + dt_bias[None, :])
    rate = -decay_rate[None, :] * delta
    cumulative = jnp.cumsum(rate, axis=0)
    along = cumulative.T
    causal = (jnp.arange(length)[:, None] >= jnp.arange(length)[None, :])[None]
    spread = along[:, :, None] - along[:, None, :]
    factor = jnp.where(causal, jnp.exp(jnp.where(causal, spread, 0.0)), 0.0) * delta.T[:, None, :]
    intersection = jnp.einsum("tgn,sgn->gts", cconv, bconv, preferred_element_type=jnp.float32)
    intersection = jnp.repeat(intersection, repeat, axis=0)
    mixing = (intersection * factor).astype(jnp.bfloat16)
    inner_out = jnp.einsum("hts,shp->thp", mixing, xconv, preferred_element_type=jnp.float32)
    tail_weight = jnp.exp(cumulative[-1][None, :] - cumulative) * delta
    weighted = (tail_weight[:, :, None] * xconv.astype(jnp.float32)).astype(jnp.bfloat16)

    cum_last = cumulative[-1]
    side = jnp.zeros((length, SIDE), jnp.bfloat16)
    side = side.at[0:3, 0:heads_here].set(jnp.stack(split3(cum_last)))
    packet = jnp.concatenate(
        [weighted.reshape(length, channels), bconv.reshape(length, local_groups * STATE), side], 1
    )
    gathered = lax.all_gather(packet, "ctx")
    blocks = gathered.shape[0]
    mine = lax.axis_index("ctx")
    w_all = gathered[:, :, :channels]
    b_all = gathered[:, :, channels : channels + local_groups * STATE]
    pieces = gathered[:, 0:3, channels + local_groups * STATE :][:, :, :heads_here].astype(
        jnp.float32
    )
    lasts = pieces[:, 0] + pieces[:, 1] + pieces[:, 2]
    order = jnp.arange(blocks)
    between = (order[:, None] < order[None, :]) & (order[None, :] < mine)
    span = jnp.sum(jnp.where(between[:, :, None], lasts[None, :, :], 0.0), axis=1)
    gain = jnp.where((order < mine)[:, None], jnp.exp(span), 0.0)
    gain = jnp.repeat(gain, HEAD_DIM, axis=1)[:, None, :]
    w_scaled = (w_all.astype(jnp.float32) * gain).reshape(blocks * length, channels)
    w_hi = w_scaled.astype(jnp.bfloat16)
    w_lo = (w_scaled - w_hi.astype(jnp.float32)).astype(jnp.bfloat16)
    b_flat = b_all.reshape(blocks * length, local_groups * STATE)
    c_flat = cconv.reshape(length, local_groups * STATE)
    scores = lax.dot_general(
        c_flat, b_flat, (((1,), (1,)), ((), ())), preferred_element_type=jnp.float32
    )
    s_hi = scores.astype(jnp.bfloat16)
    s_lo = (scores - s_hi.astype(jnp.float32)).astype(jnp.bfloat16)
    carried = (
        jnp.dot(s_hi, w_hi, preferred_element_type=jnp.float32)
        + jnp.dot(s_lo, w_hi, preferred_element_type=jnp.float32)
        + jnp.dot(s_hi, w_lo, preferred_element_type=jnp.float32)
    ).reshape(length, heads_here, HEAD_DIM)
    carried = carried * jnp.exp(cumulative)[:, :, None]
    ssm_out = inner_out + carried + d_skip[None, :, None] * xconv.astype(jnp.float32)
    gated = ssm_out.reshape(length, channels) * jax.nn.silu(z_in.astype(jnp.float32))
    norm_size = per_group * HEAD_DIM
    grouped = gated.reshape(length, local_groups, channels // local_groups)
    partial_squares = jnp.sum(grouped * grouped, axis=-1)
    if local_groups == 1:
        squares = group_sum(partial_squares, "tp", per_group // heads_here)
    else:
        squares = partial_squares
    scale = lax.rsqrt(squares / norm_size + 1e-05)
    hidden = ((grouped * scale[:, :, None]).reshape(length, channels) * norm_gain[None, :]).astype(
        jnp.bfloat16
    )
    partial_out = jnp.dot(hidden, w_out, preferred_element_type=jnp.float32)
    owners = lax.axis_size("tp")
    pieces_out = partial_out.astype(jnp.bfloat16).reshape(length, owners, -1).transpose(1, 0, 2)
    received = lax.all_to_all(pieces_out, "tp", 0, 0, tiled=True)
    summed = jnp.sum(received.astype(jnp.float32), axis=0).astype(jnp.bfloat16)
    return summed


def solution(mesh):
    return jax.shard_map(
        local,
        mesh=mesh,
        in_specs=(
            P("ctx", "tp"),
            P("ctx", "tp"),
            P("ctx", None, None),
            P("ctx", None, None),
            P(None, "tp"),
            P(),
            P("ctx", "tp"),
            P("tp"),
            P("tp"),
            P("tp"),
            P("tp"),
            P("tp", None),
        ),
        out_specs=P("ctx", "tp"),
        check_vma=False,
    )
```

```python
import jax
import jax.numpy as jnp
from jax import lax
from jax.sharding import PartitionSpec as P

HEADS = 128
HEAD_DIM = 64
STATE = 256
GROUPS = 4
CONV = 4
SIDE = 128


def shifted(block, axis, distance):
    devices = range(lax.psum(1, axis))
    route = [(i - distance, i) for i in devices if i - distance in devices]
    return lax.ppermute(block, axis, route)


def group_sum(value, axis, span):
    total = value
    step = 1
    while step < span:
        route = [(i, i ^ step) for i in range(lax.axis_size(axis))]
        total = total + lax.ppermute(total, axis, route)
        step *= 2
    return total


def causal_conv(tail, sequence, taps):
    length = sequence.shape[0]
    padded = jnp.concatenate([tail, sequence], 0).astype(jnp.float32)
    kernel = taps.astype(jnp.float32)
    total = jnp.zeros(sequence.shape, jnp.float32)
    for offset in range(taps.shape[0]):
        total = total + padded[offset : offset + length] * kernel[offset]
    return jax.nn.silu(total).astype(jnp.bfloat16)


def split3(value):
    hi = value.astype(jnp.bfloat16)
    rest = value - hi.astype(jnp.float32)
    mid = rest.astype(jnp.bfloat16)
    lo = (rest - mid.astype(jnp.float32)).astype(jnp.bfloat16)
    return hi, mid, lo


def split2(value):
    hi = value.astype(jnp.bfloat16)
    return hi, (value - hi.astype(jnp.float32)).astype(jnp.bfloat16)


def local(
    x_in, z_in, b_in, c_in, conv_x, conv_bc, dt_raw, dt_bias, decay_rate, d_skip, norm_gain, w_out
):
    length, channels = x_in.shape
    heads_here = dt_raw.shape[1]
    per_group = HEADS // GROUPS
    local_groups = max(heads_here // per_group, 1)
    repeat = heads_here // local_groups
    first_group = lax.axis_index("tp") * heads_here // per_group
    b_here = lax.dynamic_slice_in_dim(b_in, first_group, local_groups, 1).reshape(
        length, local_groups * STATE
    )
    c_here = lax.dynamic_slice_in_dim(c_in, first_group, local_groups, 1).reshape(
        length, local_groups * STATE
    )
    taps_here = lax.dynamic_slice_in_dim(conv_bc, first_group, local_groups, 2).reshape(
        CONV, 2 * local_groups * STATE
    )
    joined = jnp.concatenate([b_here, c_here], 1)
    x_tail, joined_tail = shifted(
        (x_in[length - CONV + 1 :], joined[length - CONV + 1 :]), ("cy", "cz"), 1
    )
    xconv = causal_conv(x_tail, x_in, conv_x).reshape(length, heads_here, HEAD_DIM)
    joined_conv = causal_conv(joined_tail, joined, taps_here)
    bconv = joined_conv[:, : local_groups * STATE].reshape(length, local_groups, STATE)
    cconv = joined_conv[:, local_groups * STATE :].reshape(length, local_groups, STATE)
    delta = jax.nn.softplus(dt_raw + dt_bias[None, :])
    rate = -decay_rate[None, :] * delta
    cumulative = jnp.cumsum(rate, axis=0)
    along = cumulative.T
    causal = (jnp.arange(length)[:, None] >= jnp.arange(length)[None, :])[None]
    spread = along[:, :, None] - along[:, None, :]
    factor = jnp.where(causal, jnp.exp(jnp.where(causal, spread, 0.0)), 0.0) * delta.T[:, None, :]
    intersection = jnp.einsum("tgn,sgn->gts", cconv, bconv, preferred_element_type=jnp.float32)
    intersection = jnp.repeat(intersection, repeat, axis=0)
    mixing = (intersection * factor).astype(jnp.bfloat16)
    inner_out = jnp.einsum("hts,shp->thp", mixing, xconv, preferred_element_type=jnp.float32)
    tail_weight = jnp.exp(cumulative[-1][None, :] - cumulative) * delta
    weighted = (tail_weight[:, :, None] * xconv.astype(jnp.float32)).astype(jnp.bfloat16)

    cum_last = cumulative[-1]
    side = jnp.zeros((length, SIDE), jnp.bfloat16)
    side = side.at[0:3, 0:heads_here].set(jnp.stack(split3(cum_last)))
    width = local_groups * STATE
    packet = jnp.concatenate(
        [weighted.reshape(length, channels), bconv.reshape(length, width), side], 1
    )
    gathered = lax.all_gather(packet, "cz")
    blocks = gathered.shape[0]
    mine = lax.axis_index("cz")
    w_all = gathered[:, :, :channels]
    b_flat = gathered[:, :, channels : channels + width].reshape(blocks * length, width)
    pieces = gathered[:, 0:3, channels + width :][:, :, :heads_here].astype(jnp.float32)
    lasts = pieces[:, 0] + pieces[:, 1] + pieces[:, 2]
    order = jnp.arange(blocks)
    between = (order[:, None] < order[None, :]) & (order[None, :] < mine)
    span = jnp.sum(jnp.where(between[:, :, None], lasts[None, :, :], 0.0), axis=1)
    gain = jnp.where((order < mine)[:, None], jnp.exp(span), 0.0)
    w_hi, w_lo = split2(w_all.astype(jnp.float32) * jnp.repeat(gain, HEAD_DIM, axis=1)[:, None, :])
    w_hi = w_hi.reshape(blocks * length, channels)
    w_lo = w_lo.reshape(blocks * length, channels)
    c_flat = cconv.reshape(length, width)
    scores = lax.dot_general(
        c_flat, b_flat, (((1,), (1,)), ((), ())), preferred_element_type=jnp.float32
    )
    s_hi, s_lo = split2(scores)
    carried = (
        jnp.dot(s_hi, w_hi, preferred_element_type=jnp.float32)
        + jnp.dot(s_lo, w_hi, preferred_element_type=jnp.float32)
        + jnp.dot(s_hi, w_lo, preferred_element_type=jnp.float32)
    )
    after = order[:, None] < order[None, :]
    tail = jnp.exp(jnp.sum(jnp.where(after[:, :, None], lasts[None, :, :], 0.0), axis=1))
    t_hi, t_lo = split2(w_all.astype(jnp.float32) * jnp.repeat(tail, HEAD_DIM, axis=1)[:, None, :])
    t_hi = t_hi.reshape(blocks * length, channels)
    t_lo = t_lo.reshape(blocks * length, channels)
    contract = (((0,), (0,)), ((), ()))
    row_state = lax.dot_general(
        t_hi, b_flat, contract, preferred_element_type=jnp.float32
    ) + lax.dot_general(t_lo, b_flat, contract, preferred_element_type=jnp.float32)
    row_decay = jnp.sum(lasts, axis=0)
    extra = jnp.zeros((8, width), jnp.float32).at[0, :heads_here].set(row_decay)
    rows_all = lax.all_gather(jnp.concatenate([row_state, extra], 0), "cy")
    rows = rows_all.shape[0]
    row = lax.axis_index("cy")
    states = rows_all[:, :channels]
    decays = rows_all[:, channels, :heads_here]
    order_rows = jnp.arange(rows)
    between_rows = (order_rows[:, None] < order_rows[None, :]) & (order_rows[None, :] < row)
    span_rows = jnp.sum(jnp.where(between_rows[:, :, None], decays[None, :, :], 0.0), axis=1)
    gain_rows = jnp.where((order_rows < row)[:, None], jnp.exp(span_rows), 0.0)
    entering = jnp.sum(states * jnp.repeat(gain_rows, HEAD_DIM, axis=1)[:, :, None], axis=0)
    before = jnp.sum(jnp.where((order < mine)[:, None], lasts, 0.0), axis=0)
    entering = entering * jnp.repeat(jnp.exp(before), HEAD_DIM)[:, None]
    e_hi, e_lo = split2(entering)
    contract_state = (((1,), (1,)), ((), ()))
    carried = carried + lax.dot_general(
        c_flat, e_hi, contract_state, preferred_element_type=jnp.float32
    ) + lax.dot_general(c_flat, e_lo, contract_state, preferred_element_type=jnp.float32)
    carried = carried.reshape(length, heads_here, HEAD_DIM)
    carried = carried * jnp.exp(cumulative)[:, :, None]
    ssm_out = inner_out + carried + d_skip[None, :, None] * xconv.astype(jnp.float32)
    gated = ssm_out.reshape(length, channels) * jax.nn.silu(z_in.astype(jnp.float32))
    norm_size = per_group * HEAD_DIM
    grouped = gated.reshape(length, local_groups, channels // local_groups)
    partial_squares = jnp.sum(grouped * grouped, axis=-1)
    if local_groups == 1:
        squares = group_sum(partial_squares, "tp", per_group // heads_here)
    else:
        squares = partial_squares
    scale = lax.rsqrt(squares / norm_size + 1e-05)
    hidden = ((grouped * scale[:, :, None]).reshape(length, channels) * norm_gain[None, :]).astype(
        jnp.bfloat16
    )
    partial_out = jnp.dot(hidden, w_out, preferred_element_type=jnp.float32)
    owners = lax.axis_size("tp")
    pieces_out = partial_out.astype(jnp.bfloat16).reshape(length, owners, -1).transpose(1, 0, 2)
    received = lax.all_to_all(pieces_out, "tp", 0, 0, tiled=True)
    summed = jnp.sum(received.astype(jnp.float32), axis=0).astype(jnp.bfloat16)
    return summed


def solution(mesh):
    grid = mesh.devices
    inner = 8 if grid.shape[0] % 8 == 0 else 1
    split = jax.sharding.Mesh(
        grid.reshape(grid.shape[0] // inner, inner, grid.shape[1]), ("cy", "cz", "tp")
    )
    ctx = ("cy", "cz")
    return jax.shard_map(
        local,
        mesh=split,
        in_specs=(
            P(ctx, "tp"),
            P(ctx, "tp"),
            P(ctx, None, None),
            P(ctx, None, None),
            P(None, "tp"),
            P(),
            P(ctx, "tp"),
            P("tp"),
            P("tp"),
            P("tp"),
            P("tp"),
            P("tp", None),
        ),
        out_specs=P(ctx, "tp"),
        check_vma=False,
    )
```

```python
import jax
import jax.numpy as jnp
from jax import lax
from jax.sharding import PartitionSpec as P

HEADS = 128
HEAD_DIM = 64
STATE = 256
GROUPS = 4
CONV = 4
SIDE = 128


def shifted(block, axis, distance):
    devices = range(lax.psum(1, axis))
    route = [(i - distance, i) for i in devices if i - distance in devices]
    return lax.ppermute(block, axis, route)


def group_sum(value, axis, span):
    total = value
    step = 1
    while step < span:
        route = [(i, i ^ step) for i in range(lax.axis_size(axis))]
        total = total + lax.ppermute(total, axis, route)
        step *= 2
    return total


def causal_conv(tail, sequence, taps):
    length = sequence.shape[0]
    padded = jnp.concatenate([tail, sequence], 0).astype(jnp.float32)
    kernel = taps.astype(jnp.float32)
    total = jnp.zeros(sequence.shape, jnp.float32)
    for offset in range(taps.shape[0]):
        total = total + padded[offset : offset + length] * kernel[offset]
    return jax.nn.silu(total).astype(jnp.bfloat16)


def split3(value):
    hi = value.astype(jnp.bfloat16)
    rest = value - hi.astype(jnp.float32)
    mid = rest.astype(jnp.bfloat16)
    lo = (rest - mid.astype(jnp.float32)).astype(jnp.bfloat16)
    return hi, mid, lo


def split2(value):
    hi = value.astype(jnp.bfloat16)
    return hi, (value - hi.astype(jnp.float32)).astype(jnp.bfloat16)


def local(
    x_in, z_in, b_in, c_in, conv_x, conv_bc, dt_raw, dt_bias, decay_rate, d_skip, norm_gain, w_out
):
    length, channels = x_in.shape
    heads_here = dt_raw.shape[1]
    per_group = HEADS // GROUPS
    local_groups = max(heads_here // per_group, 1)
    repeat = heads_here // local_groups
    first_group = lax.axis_index("tp") * heads_here // per_group
    b_here = lax.dynamic_slice_in_dim(b_in, first_group, local_groups, 1).reshape(
        length, local_groups * STATE
    )
    c_here = lax.dynamic_slice_in_dim(c_in, first_group, local_groups, 1).reshape(
        length, local_groups * STATE
    )
    taps_here = lax.dynamic_slice_in_dim(conv_bc, first_group, local_groups, 2).reshape(
        CONV, 2 * local_groups * STATE
    )
    joined = jnp.concatenate([b_here, c_here], 1)
    x_tail, joined_tail = shifted(
        (x_in[length - CONV + 1 :], joined[length - CONV + 1 :]), ("cy", "cz"), 1
    )
    xconv = causal_conv(x_tail, x_in, conv_x).reshape(length, heads_here, HEAD_DIM)
    joined_conv = causal_conv(joined_tail, joined, taps_here)
    bconv = joined_conv[:, : local_groups * STATE].reshape(length, local_groups, STATE)
    cconv = joined_conv[:, local_groups * STATE :].reshape(length, local_groups, STATE)
    delta = jax.nn.softplus(dt_raw + dt_bias[None, :])
    rate = -decay_rate[None, :] * delta
    cumulative = jnp.cumsum(rate, axis=0)
    along = cumulative.T
    causal = (jnp.arange(length)[:, None] >= jnp.arange(length)[None, :])[None]
    spread = along[:, :, None] - along[:, None, :]
    factor = jnp.where(causal, jnp.exp(jnp.where(causal, spread, 0.0)), 0.0) * delta.T[:, None, :]
    intersection = jnp.einsum("tgn,sgn->gts", cconv, bconv, preferred_element_type=jnp.float32)
    intersection = jnp.repeat(intersection, repeat, axis=0)
    mixing = (intersection * factor).astype(jnp.bfloat16)
    inner_out = jnp.einsum("hts,shp->thp", mixing, xconv, preferred_element_type=jnp.float32)
    tail_weight = jnp.exp(cumulative[-1][None, :] - cumulative) * delta
    weighted = (tail_weight[:, :, None] * xconv.astype(jnp.float32)).astype(jnp.bfloat16)

    cum_last = cumulative[-1]
    side = jnp.zeros((length, SIDE), jnp.bfloat16)
    side = side.at[0:3, 0:heads_here].set(jnp.stack(split3(cum_last)))
    width = local_groups * STATE
    packet = jnp.concatenate(
        [weighted.reshape(length, channels), bconv.reshape(length, width), side], 1
    )
    gathered = lax.all_gather(packet, "cz")
    blocks = gathered.shape[0]
    mine = lax.axis_index("cz")
    w_all = gathered[:, :, :channels]
    b_flat = gathered[:, :, channels : channels + width].reshape(blocks * length, width)
    pieces = gathered[:, 0:3, channels + width :][:, :, :heads_here].astype(jnp.float32)
    lasts = pieces[:, 0] + pieces[:, 1] + pieces[:, 2]
    order = jnp.arange(blocks)
    between = (order[:, None] < order[None, :]) & (order[None, :] < mine)
    span = jnp.sum(jnp.where(between[:, :, None], lasts[None, :, :], 0.0), axis=1)
    gain = jnp.where((order < mine)[:, None], jnp.exp(span), 0.0)
    w_hi, w_lo = split2(w_all.astype(jnp.float32) * jnp.repeat(gain, HEAD_DIM, axis=1)[:, None, :])
    w_hi = w_hi.reshape(blocks * length, channels)
    w_lo = w_lo.reshape(blocks * length, channels)
    c_flat = cconv.reshape(length, width)
    scores = lax.dot_general(
        c_flat, b_flat, (((1,), (1,)), ((), ())), preferred_element_type=jnp.float32
    )
    s_hi, s_lo = split2(scores)
    carried = (
        jnp.dot(s_hi, w_hi, preferred_element_type=jnp.float32)
        + jnp.dot(s_lo, w_hi, preferred_element_type=jnp.float32)
        + jnp.dot(s_hi, w_lo, preferred_element_type=jnp.float32)
    )
    after = order[:, None] < order[None, :]
    tail = jnp.exp(jnp.sum(jnp.where(after[:, :, None], lasts[None, :, :], 0.0), axis=1))
    t_hi, t_lo = split2(w_all.astype(jnp.float32) * jnp.repeat(tail, HEAD_DIM, axis=1)[:, None, :])
    t_hi = t_hi.reshape(blocks * length, channels)
    t_lo = t_lo.reshape(blocks * length, channels)
    contract = (((0,), (0,)), ((), ()))
    row_state = lax.dot_general(
        t_hi, b_flat, contract, preferred_element_type=jnp.float32
    ) + lax.dot_general(t_lo, b_flat, contract, preferred_element_type=jnp.float32)
    row_decay = jnp.sum(lasts, axis=0)
    extra = jnp.zeros((8, width), jnp.float32).at[0, :heads_here].set(row_decay)
    rows_all = lax.all_gather(jnp.concatenate([row_state, extra], 0), "cy")
    rows = rows_all.shape[0]
    row = lax.axis_index("cy")
    states = rows_all[:, :channels]
    decays = rows_all[:, channels, :heads_here]
    order_rows = jnp.arange(rows)
    between_rows = (order_rows[:, None] < order_rows[None, :]) & (order_rows[None, :] < row)
    span_rows = jnp.sum(jnp.where(between_rows[:, :, None], decays[None, :, :], 0.0), axis=1)
    gain_rows = jnp.where((order_rows < row)[:, None], jnp.exp(span_rows), 0.0)
    entering = jnp.sum(states * jnp.repeat(gain_rows, HEAD_DIM, axis=1)[:, :, None], axis=0)
    before = jnp.sum(jnp.where((order < mine)[:, None], lasts, 0.0), axis=0)
    entering = entering * jnp.repeat(jnp.exp(before), HEAD_DIM)[:, None]
    e_hi, e_lo = split2(entering)
    contract_state = (((1,), (1,)), ((), ()))
    carried = carried + lax.dot_general(
        c_flat, e_hi, contract_state, preferred_element_type=jnp.float32
    ) + lax.dot_general(c_flat, e_lo, contract_state, preferred_element_type=jnp.float32)
    carried = carried.reshape(length, heads_here, HEAD_DIM)
    carried = carried * jnp.exp(cumulative)[:, :, None]
    ssm_out = inner_out + carried + d_skip[None, :, None] * xconv.astype(jnp.float32)
    gated = ssm_out.reshape(length, channels) * jax.nn.silu(z_in.astype(jnp.float32))
    norm_size = per_group * HEAD_DIM
    grouped = gated.reshape(length, local_groups, channels // local_groups)
    partial_squares = jnp.sum(grouped * grouped, axis=-1)
    if local_groups == 1:
        squares = group_sum(partial_squares, "tp", per_group // heads_here)
    else:
        squares = partial_squares
    scale = lax.rsqrt(squares / norm_size + 1e-05)
    hidden = ((grouped * scale[:, :, None]).reshape(length, channels) * norm_gain[None, :]).astype(
        jnp.bfloat16
    )
    partial_out = jnp.dot(hidden, w_out, preferred_element_type=jnp.float32)
    owners = lax.psum(1, "tp")
    own = lax.axis_index("tp")
    pieces_out = partial_out.astype(jnp.bfloat16).reshape(length, owners, -1).transpose(1, 0, 2)
    total = lax.dynamic_index_in_dim(pieces_out, own, 0, keepdims=False).astype(jnp.float32)
    for k in range(1, owners):
        route = [(i, (i + k) % owners) for i in range(owners)]
        piece = lax.dynamic_index_in_dim(pieces_out, (own + k) % owners, 0, keepdims=False)
        total = total + lax.ppermute(piece, "tp", route).astype(jnp.float32)
    summed = total.astype(jnp.bfloat16)
    return summed


def solution(mesh):
    grid = mesh.devices
    inner = 8 if grid.shape[0] % 8 == 0 else 1
    split = jax.sharding.Mesh(
        grid.reshape(grid.shape[0] // inner, inner, grid.shape[1]), ("cy", "cz", "tp")
    )
    ctx = ("cy", "cz")
    return jax.shard_map(
        local,
        mesh=split,
        in_specs=(
            P(ctx, "tp"),
            P(ctx, "tp"),
            P(ctx, None, None),
            P(ctx, None, None),
            P(None, "tp"),
            P(),
            P(ctx, "tp"),
            P("tp"),
            P("tp"),
            P("tp"),
            P("tp"),
            P("tp", None),
        ),
        out_specs=P(ctx, "tp"),
        check_vma=False,
    )
```

```python
import jax
import jax.numpy as jnp
from jax import lax
from jax.sharding import PartitionSpec as P

HEADS = 128
HEAD_DIM = 64
STATE = 256
GROUPS = 4
CONV = 4
SIDE = 128


def shifted(block, axis, distance):
    devices = range(lax.psum(1, axis))
    route = [(i - distance, i) for i in devices if i - distance in devices]
    return lax.ppermute(block, axis, route)


def group_sum(value, axis, span):
    total = value
    step = 1
    while step < span:
        route = [(i, i ^ step) for i in range(lax.axis_size(axis))]
        total = total + lax.ppermute(total, axis, route)
        step *= 2
    return total


def causal_conv(tail, sequence, taps):
    length = sequence.shape[0]
    padded = jnp.concatenate([tail, sequence], 0).astype(jnp.float32)
    kernel = taps.astype(jnp.float32)
    total = jnp.zeros(sequence.shape, jnp.float32)
    for offset in range(taps.shape[0]):
        total = total + padded[offset : offset + length] * kernel[offset]
    return jax.nn.silu(total).astype(jnp.bfloat16)


def split3(value):
    hi = value.astype(jnp.bfloat16)
    rest = value - hi.astype(jnp.float32)
    mid = rest.astype(jnp.bfloat16)
    lo = (rest - mid.astype(jnp.float32)).astype(jnp.bfloat16)
    return hi, mid, lo


def split2(value):
    hi = value.astype(jnp.bfloat16)
    return hi, (value - hi.astype(jnp.float32)).astype(jnp.bfloat16)


def local(
    x_in, z_in, b_in, c_in, conv_x, conv_bc, dt_raw, dt_bias, decay_rate, d_skip, norm_gain, w_out
):
    length, channels = x_in.shape
    heads_here = dt_raw.shape[1]
    per_group = HEADS // GROUPS
    local_groups = max(heads_here // per_group, 1)
    repeat = heads_here // local_groups
    first_group = lax.axis_index("tp") * heads_here // per_group
    b_here = lax.dynamic_slice_in_dim(b_in, first_group, local_groups, 1).reshape(
        length, local_groups * STATE
    )
    c_here = lax.dynamic_slice_in_dim(c_in, first_group, local_groups, 1).reshape(
        length, local_groups * STATE
    )
    taps_here = lax.dynamic_slice_in_dim(conv_bc, first_group, local_groups, 2).reshape(
        CONV, 2 * local_groups * STATE
    )
    joined = jnp.concatenate([b_here, c_here], 1)
    x_tail, joined_tail = shifted(
        (x_in[length - CONV + 1 :], joined[length - CONV + 1 :]), ("cy", "cz"), 1
    )
    xconv = causal_conv(x_tail, x_in, conv_x).reshape(length, heads_here, HEAD_DIM)
    joined_conv = causal_conv(joined_tail, joined, taps_here)
    bconv = joined_conv[:, : local_groups * STATE].reshape(length, local_groups, STATE)
    cconv = joined_conv[:, local_groups * STATE :].reshape(length, local_groups, STATE)
    delta = jax.nn.softplus(dt_raw + dt_bias[None, :])
    rate = -decay_rate[None, :] * delta
    cumulative = jnp.cumsum(rate, axis=0)
    along = cumulative.T
    causal = (jnp.arange(length)[:, None] >= jnp.arange(length)[None, :])[None]
    spread = along[:, :, None] - along[:, None, :]
    factor = jnp.where(causal, jnp.exp(jnp.where(causal, spread, 0.0)), 0.0) * delta.T[:, None, :]
    intersection = jnp.einsum("tgn,sgn->gts", cconv, bconv, preferred_element_type=jnp.float32)
    intersection = jnp.repeat(intersection, repeat, axis=0)
    mixing = (intersection * factor).astype(jnp.bfloat16)
    inner_out = jnp.einsum("hts,shp->thp", mixing, xconv, preferred_element_type=jnp.float32)
    tail_weight = jnp.exp(cumulative[-1][None, :] - cumulative) * delta
    weighted = (tail_weight[:, :, None] * xconv.astype(jnp.float32)).astype(jnp.bfloat16)

    cum_last = cumulative[-1]
    side = jnp.zeros((length, SIDE), jnp.bfloat16)
    side = side.at[0:3, 0:heads_here].set(jnp.stack(split3(cum_last)))
    width = local_groups * STATE
    packet = jnp.concatenate(
        [weighted.reshape(length, channels), bconv.reshape(length, width), side], 1
    )
    gathered = lax.all_gather(packet, "cz")
    blocks = gathered.shape[0]
    mine = lax.axis_index("cz")
    w_all = gathered[:, :, :channels]
    b_flat = gathered[:, :, channels : channels + width].reshape(blocks * length, width)
    pieces = gathered[:, 0:3, channels + width :][:, :, :heads_here].astype(jnp.float32)
    lasts = pieces[:, 0] + pieces[:, 1] + pieces[:, 2]
    order = jnp.arange(blocks)
    between = (order[:, None] < order[None, :]) & (order[None, :] < mine)
    span = jnp.sum(jnp.where(between[:, :, None], lasts[None, :, :], 0.0), axis=1)
    gain = jnp.where((order < mine)[:, None], jnp.exp(span), 0.0)
    w_hi, w_lo = split2(w_all.astype(jnp.float32) * jnp.repeat(gain, HEAD_DIM, axis=1)[:, None, :])
    w_hi = w_hi.reshape(blocks * length, channels)
    w_lo = w_lo.reshape(blocks * length, channels)
    c_flat = cconv.reshape(length, width)
    scores = lax.dot_general(
        c_flat, b_flat, (((1,), (1,)), ((), ())), preferred_element_type=jnp.float32
    )
    s_hi, s_lo = split2(scores)
    carried = (
        jnp.dot(s_hi, w_hi, preferred_element_type=jnp.float32)
        + jnp.dot(s_lo, w_hi, preferred_element_type=jnp.float32)
        + jnp.dot(s_hi, w_lo, preferred_element_type=jnp.float32)
    )
    after = order[:, None] < order[None, :]
    tail = jnp.exp(jnp.sum(jnp.where(after[:, :, None], lasts[None, :, :], 0.0), axis=1))
    t_hi, t_lo = split2(w_all.astype(jnp.float32) * jnp.repeat(tail, HEAD_DIM, axis=1)[:, None, :])
    t_hi = t_hi.reshape(blocks * length, channels)
    t_lo = t_lo.reshape(blocks * length, channels)
    contract = (((0,), (0,)), ((), ()))
    row_state = lax.dot_general(
        t_hi, b_flat, contract, preferred_element_type=jnp.float32
    ) + lax.dot_general(t_lo, b_flat, contract, preferred_element_type=jnp.float32)
    row_decay = jnp.sum(lasts, axis=0)
    extra = jnp.zeros((8, width), jnp.float32).at[0, :heads_here].set(row_decay)
    rows_all = lax.all_gather(jnp.concatenate([row_state, extra], 0), "cy")
    rows = rows_all.shape[0]
    row = lax.axis_index("cy")
    states = rows_all[:, :channels]
    decays = rows_all[:, channels, :heads_here]
    order_rows = jnp.arange(rows)
    between_rows = (order_rows[:, None] < order_rows[None, :]) & (order_rows[None, :] < row)
    span_rows = jnp.sum(jnp.where(between_rows[:, :, None], decays[None, :, :], 0.0), axis=1)
    gain_rows = jnp.where((order_rows < row)[:, None], jnp.exp(span_rows), 0.0)
    entering = jnp.sum(states * jnp.repeat(gain_rows, HEAD_DIM, axis=1)[:, :, None], axis=0)
    before = jnp.sum(jnp.where((order < mine)[:, None], lasts, 0.0), axis=0)
    entering = entering * jnp.repeat(jnp.exp(before), HEAD_DIM)[:, None]
    e_hi, e_lo = split2(entering)
    contract_state = (((1,), (1,)), ((), ()))
    carried = carried + lax.dot_general(
        c_flat, e_hi, contract_state, preferred_element_type=jnp.float32
    ) + lax.dot_general(c_flat, e_lo, contract_state, preferred_element_type=jnp.float32)
    carried = carried.reshape(length, heads_here, HEAD_DIM)
    carried = carried * jnp.exp(cumulative)[:, :, None]
    ssm_out = inner_out + carried + d_skip[None, :, None] * xconv.astype(jnp.float32)
    gated = ssm_out.reshape(length, channels) * jax.nn.silu(z_in.astype(jnp.float32))
    norm_size = per_group * HEAD_DIM
    owners = lax.psum(1, "tp")
    span_tp = per_group // heads_here
    partial_squares = jnp.sum(gated * gated, axis=-1)
    unscaled = (gated * norm_gain[None, :]).astype(jnp.bfloat16)
    partial_out = jnp.dot(unscaled, w_out, preferred_element_type=jnp.float32)
    pieces_out = partial_out.astype(jnp.bfloat16).reshape(length, owners, -1).transpose(1, 0, 2)
    sq_block = jnp.zeros((length, SIDE), jnp.bfloat16)
    sq_block = sq_block.at[:, 0:3].set(jnp.stack(split3(partial_squares), axis=1))
    send = jnp.concatenate(
        [pieces_out, jnp.broadcast_to(sq_block[None], (owners, length, SIDE))], axis=2
    )
    received = lax.all_to_all(send, "tp", 0, 0, tiled=True)
    cols = pieces_out.shape[2]
    parts = received[:, :, :cols].astype(jnp.float32)
    sq = received[:, :, cols : cols + 3].astype(jnp.float32)
    src_squares = sq[:, :, 0] + sq[:, :, 1] + sq[:, :, 2]
    group_squares = jnp.sum(src_squares.reshape(owners // span_tp, span_tp, length), axis=1)
    scale = lax.rsqrt(group_squares / norm_size + 1e-05)
    scale_src = jnp.repeat(scale, span_tp, axis=0)
    summed = jnp.sum(parts * scale_src[:, :, None], axis=0).astype(jnp.bfloat16)
    return summed


def solution(mesh):
    grid = mesh.devices
    inner = 8 if grid.shape[0] % 8 == 0 else 1
    split = jax.sharding.Mesh(
        grid.reshape(grid.shape[0] // inner, inner, grid.shape[1]), ("cy", "cz", "tp")
    )
    ctx = ("cy", "cz")
    return jax.shard_map(
        local,
        mesh=split,
        in_specs=(
            P(ctx, "tp"),
            P(ctx, "tp"),
            P(ctx, None, None),
            P(ctx, None, None),
            P(None, "tp"),
            P(),
            P(ctx, "tp"),
            P("tp"),
            P("tp"),
            P("tp"),
            P("tp"),
            P("tp", None),
        ),
        out_specs=P(ctx, "tp"),
        check_vma=False,
    )
```

```python
import jax
import jax.numpy as jnp
from jax import lax
from jax.sharding import PartitionSpec as P

HEADS = 128
HEAD_DIM = 64
STATE = 256
GROUPS = 4
CONV = 4
SIDE = 128


def shifted(block, axis, distance):
    devices = range(lax.psum(1, axis))
    route = [(i - distance, i) for i in devices if i - distance in devices]
    return lax.ppermute(block, axis, route)


def group_sum(value, axis, span):
    total = value
    step = 1
    while step < span:
        route = [(i, i ^ step) for i in range(lax.axis_size(axis))]
        total = total + lax.ppermute(total, axis, route)
        step *= 2
    return total


def causal_conv(tail, sequence, taps):
    length = sequence.shape[0]
    padded = jnp.concatenate([tail, sequence], 0).astype(jnp.float32)
    kernel = taps.astype(jnp.float32)
    total = jnp.zeros(sequence.shape, jnp.float32)
    for offset in range(taps.shape[0]):
        total = total + padded[offset : offset + length] * kernel[offset]
    return jax.nn.silu(total).astype(jnp.bfloat16)


def split3(value):
    hi = value.astype(jnp.bfloat16)
    rest = value - hi.astype(jnp.float32)
    mid = rest.astype(jnp.bfloat16)
    lo = (rest - mid.astype(jnp.float32)).astype(jnp.bfloat16)
    return hi, mid, lo


def split2(value):
    hi = value.astype(jnp.bfloat16)
    return hi, (value - hi.astype(jnp.float32)).astype(jnp.bfloat16)


def local(
    x_in, z_in, b_in, c_in, conv_x, conv_bc, dt_raw, dt_bias, decay_rate, d_skip, norm_gain, w_out
):
    length, channels = x_in.shape
    heads_here = dt_raw.shape[1]
    per_group = HEADS // GROUPS
    local_groups = max(heads_here // per_group, 1)
    repeat = heads_here // local_groups
    first_group = lax.axis_index("tp") * heads_here // per_group
    b_here = lax.dynamic_slice_in_dim(b_in, first_group, local_groups, 1).reshape(
        length, local_groups * STATE
    )
    c_here = lax.dynamic_slice_in_dim(c_in, first_group, local_groups, 1).reshape(
        length, local_groups * STATE
    )
    taps_here = lax.dynamic_slice_in_dim(conv_bc, first_group, local_groups, 2).reshape(
        CONV, 2 * local_groups * STATE
    )
    joined = jnp.concatenate([b_here, c_here], 1)
    x_tail, joined_tail = shifted(
        (x_in[length - CONV + 1 :], joined[length - CONV + 1 :]), ("cy", "cz"), 1
    )
    xconv = causal_conv(x_tail, x_in, conv_x).reshape(length, heads_here, HEAD_DIM)
    joined_conv = causal_conv(joined_tail, joined, taps_here)
    bconv = joined_conv[:, : local_groups * STATE].reshape(length, local_groups, STATE)
    cconv = joined_conv[:, local_groups * STATE :].reshape(length, local_groups, STATE)
    delta = jax.nn.softplus(dt_raw + dt_bias[None, :])
    rate = -decay_rate[None, :] * delta
    cumulative = jnp.cumsum(rate, axis=0)
    along = cumulative.T
    causal = (jnp.arange(length)[:, None] >= jnp.arange(length)[None, :])[None]
    spread = along[:, :, None] - along[:, None, :]
    factor = jnp.where(causal, jnp.exp(jnp.where(causal, spread, 0.0)), 0.0) * delta.T[:, None, :]
    intersection = jnp.einsum("tgn,sgn->gts", cconv, bconv, preferred_element_type=jnp.float32)
    intersection = jnp.repeat(intersection, repeat, axis=0)
    mixing = (intersection * factor).astype(jnp.bfloat16)
    inner_out = jnp.einsum("hts,shp->thp", mixing, xconv, preferred_element_type=jnp.float32)
    tail_weight = jnp.exp(cumulative[-1][None, :] - cumulative) * delta
    weighted = (tail_weight[:, :, None] * xconv.astype(jnp.float32)).astype(jnp.bfloat16)

    cum_last = cumulative[-1]
    side = jnp.zeros((length, SIDE), jnp.bfloat16)
    side = side.at[0:3, 0:heads_here].set(jnp.stack(split3(cum_last)))
    width = local_groups * STATE
    packet = jnp.concatenate(
        [weighted.reshape(length, channels), bconv.reshape(length, width), side], 1
    )
    gathered = lax.all_gather(packet, "cz")
    blocks = gathered.shape[0]
    mine = lax.axis_index("cz")
    w_all = gathered[:, :, :channels]
    b_flat = gathered[:, :, channels : channels + width].reshape(blocks * length, width)
    pieces = gathered[:, 0:3, channels + width :][:, :, :heads_here].astype(jnp.float32)
    lasts = pieces[:, 0] + pieces[:, 1] + pieces[:, 2]
    order = jnp.arange(blocks)
    between = (order[:, None] < order[None, :]) & (order[None, :] < mine)
    span = jnp.sum(jnp.where(between[:, :, None], lasts[None, :, :], 0.0), axis=1)
    gain = jnp.where((order < mine)[:, None], jnp.exp(span), 0.0)
    w_hi, w_lo = split2(w_all.astype(jnp.float32) * jnp.repeat(gain, HEAD_DIM, axis=1)[:, None, :])
    w_hi = w_hi.reshape(blocks * length, channels)
    w_lo = w_lo.reshape(blocks * length, channels)
    c_flat = cconv.reshape(length, width)
    scores = lax.dot_general(
        c_flat, b_flat, (((1,), (1,)), ((), ())), preferred_element_type=jnp.float32
    )
    s_hi, s_lo = split2(scores)
    carried = (
        jnp.dot(s_hi, w_hi, preferred_element_type=jnp.float32)
        + jnp.dot(s_lo, w_hi, preferred_element_type=jnp.float32)
        + jnp.dot(s_hi, w_lo, preferred_element_type=jnp.float32)
    )
    after = order[:, None] < order[None, :]
    tail = jnp.exp(jnp.sum(jnp.where(after[:, :, None], lasts[None, :, :], 0.0), axis=1))
    t_hi, t_lo = split2(w_all.astype(jnp.float32) * jnp.repeat(tail, HEAD_DIM, axis=1)[:, None, :])
    t_hi = t_hi.reshape(blocks * length, channels)
    t_lo = t_lo.reshape(blocks * length, channels)
    contract = (((0,), (0,)), ((), ()))
    row_state = lax.dot_general(
        t_hi, b_flat, contract, preferred_element_type=jnp.float32
    ) + lax.dot_general(t_lo, b_flat, contract, preferred_element_type=jnp.float32)
    row_decay = jnp.sum(lasts, axis=0)
    extra = jnp.zeros((8, width), jnp.float32).at[0, :heads_here].set(row_decay)
    rows_all = lax.all_gather(jnp.concatenate([row_state, extra], 0), "cy")
    rows = rows_all.shape[0]
    row = lax.axis_index("cy")
    states = rows_all[:, :channels]
    decays = rows_all[:, channels, :heads_here]
    order_rows = jnp.arange(rows)
    between_rows = (order_rows[:, None] < order_rows[None, :]) & (order_rows[None, :] < row)
    span_rows = jnp.sum(jnp.where(between_rows[:, :, None], decays[None, :, :], 0.0), axis=1)
    gain_rows = jnp.where((order_rows < row)[:, None], jnp.exp(span_rows), 0.0)
    entering = jnp.sum(states * jnp.repeat(gain_rows, HEAD_DIM, axis=1)[:, :, None], axis=0)
    before = jnp.sum(jnp.where((order < mine)[:, None], lasts, 0.0), axis=0)
    entering = entering * jnp.repeat(jnp.exp(before), HEAD_DIM)[:, None]
    e_hi, e_lo = split2(entering)
    contract_state = (((1,), (1,)), ((), ()))
    carried = carried + lax.dot_general(
        c_flat, e_hi, contract_state, preferred_element_type=jnp.float32
    ) + lax.dot_general(c_flat, e_lo, contract_state, preferred_element_type=jnp.float32)
    carried = carried.reshape(length, heads_here, HEAD_DIM)
    carried = carried * jnp.exp(cumulative)[:, :, None]
    ssm_out = inner_out + carried + d_skip[None, :, None] * xconv.astype(jnp.float32)
    gated = ssm_out.reshape(length, channels) * jax.nn.silu(z_in.astype(jnp.float32))
    norm_size = per_group * HEAD_DIM
    owners = lax.psum(1, "tp")
    span_tp = per_group // heads_here
    partial_squares = jnp.sum(gated * gated, axis=-1)
    unscaled = (gated * norm_gain[None, :]).astype(jnp.bfloat16)
    partial_out = jnp.dot(unscaled, w_out, preferred_element_type=jnp.float32)
    pieces_out = partial_out.astype(jnp.bfloat16).reshape(length, owners, -1).transpose(1, 0, 2)
    cols = pieces_out.shape[2]
    sq_row = jnp.zeros((cols,), jnp.bfloat16).at[: 3 * length].set(
        jnp.concatenate(split3(partial_squares))
    )
    send = jnp.concatenate(
        [pieces_out, jnp.broadcast_to(sq_row[None, None], (owners, 1, cols))], axis=1
    )
    received = lax.all_to_all(send, "tp", 0, 0, tiled=True)
    parts = received[:, :length].astype(jnp.float32)
    sq = received[:, length, : 3 * length].astype(jnp.float32)
    src_squares = sq[:, :length] + sq[:, length : 2 * length] + sq[:, 2 * length :]
    group_squares = jnp.sum(src_squares.reshape(owners // span_tp, span_tp, length), axis=1)
    scale = lax.rsqrt(group_squares / norm_size + 1e-05)
    scale_src = jnp.repeat(scale, span_tp, axis=0)
    summed = jnp.sum(parts * scale_src[:, :, None], axis=0).astype(jnp.bfloat16)
    return summed


def solution(mesh):
    grid = mesh.devices
    inner = 8 if grid.shape[0] % 8 == 0 else 1
    split = jax.sharding.Mesh(
        grid.reshape(grid.shape[0] // inner, inner, grid.shape[1]), ("cy", "cz", "tp")
    )
    ctx = ("cy", "cz")
    return jax.shard_map(
        local,
        mesh=split,
        in_specs=(
            P(ctx, "tp"),
            P(ctx, "tp"),
            P(ctx, None, None),
            P(ctx, None, None),
            P(None, "tp"),
            P(),
            P(ctx, "tp"),
            P("tp"),
            P("tp"),
            P("tp"),
            P("tp"),
            P("tp", None),
        ),
        out_specs=P(ctx, "tp"),
        check_vma=False,
    )
```

```python
import jax
import jax.numpy as jnp
from jax import lax
from jax.sharding import PartitionSpec as P

HEADS = 128
HEAD_DIM = 64
STATE = 256
GROUPS = 4
CONV = 4
SIDE = 128


def shifted(block, axis, distance):
    devices = range(lax.psum(1, axis))
    route = [(i - distance, i) for i in devices if i - distance in devices]
    return lax.ppermute(block, axis, route)


def group_sum(value, axis, span):
    total = value
    step = 1
    while step < span:
        route = [(i, i ^ step) for i in range(lax.axis_size(axis))]
        total = total + lax.ppermute(total, axis, route)
        step *= 2
    return total


def causal_conv(tail, sequence, taps):
    length = sequence.shape[0]
    padded = jnp.concatenate([tail, sequence], 0).astype(jnp.float32)
    kernel = taps.astype(jnp.float32)
    total = jnp.zeros(sequence.shape, jnp.float32)
    for offset in range(taps.shape[0]):
        total = total + padded[offset : offset + length] * kernel[offset]
    return jax.nn.silu(total).astype(jnp.bfloat16)


def split3(value):
    hi = value.astype(jnp.bfloat16)
    rest = value - hi.astype(jnp.float32)
    mid = rest.astype(jnp.bfloat16)
    lo = (rest - mid.astype(jnp.float32)).astype(jnp.bfloat16)
    return hi, mid, lo


def split2(value):
    hi = value.astype(jnp.bfloat16)
    return hi, (value - hi.astype(jnp.float32)).astype(jnp.bfloat16)


def local(
    x_in, z_in, b_in, c_in, conv_x, conv_bc, dt_raw, dt_bias, decay_rate, d_skip, norm_gain, w_out
):
    length, channels = x_in.shape
    heads_here = dt_raw.shape[1]
    per_group = HEADS // GROUPS
    local_groups = max(heads_here // per_group, 1)
    repeat = heads_here // local_groups
    first_group = lax.axis_index("tp") * heads_here // per_group
    b_here = lax.dynamic_slice_in_dim(b_in, first_group, local_groups, 1).reshape(
        length, local_groups * STATE
    )
    c_here = lax.dynamic_slice_in_dim(c_in, first_group, local_groups, 1).reshape(
        length, local_groups * STATE
    )
    taps_here = lax.dynamic_slice_in_dim(conv_bc, first_group, local_groups, 2).reshape(
        CONV, 2 * local_groups * STATE
    )
    joined = jnp.concatenate([b_here, c_here], 1)
    x_tail, joined_tail = shifted(
        (x_in[length - CONV + 1 :], joined[length - CONV + 1 :]), ("cy", "cz"), 1
    )
    xconv = causal_conv(x_tail, x_in, conv_x).reshape(length, heads_here, HEAD_DIM)
    joined_conv = causal_conv(joined_tail, joined, taps_here)
    bconv = joined_conv[:, : local_groups * STATE].reshape(length, local_groups, STATE)
    cconv = joined_conv[:, local_groups * STATE :].reshape(length, local_groups, STATE)
    delta = jax.nn.softplus(dt_raw + dt_bias[None, :])
    rate = -decay_rate[None, :] * delta
    cumulative = jnp.cumsum(rate, axis=0)
    along = cumulative.T
    causal = (jnp.arange(length)[:, None] >= jnp.arange(length)[None, :])[None]
    spread = along[:, :, None] - along[:, None, :]
    factor = jnp.where(causal, jnp.exp(jnp.where(causal, spread, 0.0)), 0.0) * delta.T[:, None, :]
    intersection = jnp.einsum("tgn,sgn->gts", cconv, bconv, preferred_element_type=jnp.float32)
    intersection = jnp.repeat(intersection, repeat, axis=0)
    mixing = (intersection * factor).astype(jnp.bfloat16)
    inner_out = jnp.einsum("hts,shp->thp", mixing, xconv, preferred_element_type=jnp.float32)
    tail_weight = jnp.exp(cumulative[-1][None, :] - cumulative) * delta
    weighted = (tail_weight[:, :, None] * xconv.astype(jnp.float32)).astype(jnp.bfloat16)

    cum_last = cumulative[-1]
    width = local_groups * STATE
    side = jnp.zeros((channels + width,), jnp.bfloat16)
    side = side.at[: 3 * heads_here].set(jnp.concatenate(split3(cum_last)))
    packet = jnp.concatenate(
        [weighted.reshape(length, channels), bconv.reshape(length, width)], 1
    )
    packet = jnp.concatenate([packet, side[None]], 0)
    gathered = lax.all_gather(packet, "cz")
    blocks = gathered.shape[0]
    mine = lax.axis_index("cz")
    w_all = gathered[:, :length, :channels]
    b_flat = gathered[:, :length, channels : channels + width].reshape(blocks * length, width)
    pieces = gathered[:, length, : 3 * heads_here].astype(jnp.float32)
    pieces = pieces.reshape(blocks, 3, heads_here)
    lasts = pieces[:, 0] + pieces[:, 1] + pieces[:, 2]
    order = jnp.arange(blocks)
    between = (order[:, None] < order[None, :]) & (order[None, :] < mine)
    span = jnp.sum(jnp.where(between[:, :, None], lasts[None, :, :], 0.0), axis=1)
    gain = jnp.where((order < mine)[:, None], jnp.exp(span), 0.0)
    w_hi, w_lo = split2(w_all.astype(jnp.float32) * jnp.repeat(gain, HEAD_DIM, axis=1)[:, None, :])
    w_hi = w_hi.reshape(blocks * length, channels)
    w_lo = w_lo.reshape(blocks * length, channels)
    c_flat = cconv.reshape(length, width)
    scores = lax.dot_general(
        c_flat, b_flat, (((1,), (1,)), ((), ())), preferred_element_type=jnp.float32
    )
    s_hi, s_lo = split2(scores)
    carried = (
        jnp.dot(s_hi, w_hi, preferred_element_type=jnp.float32)
        + jnp.dot(s_lo, w_hi, preferred_element_type=jnp.float32)
        + jnp.dot(s_hi, w_lo, preferred_element_type=jnp.float32)
    )
    after = order[:, None] < order[None, :]
    tail = jnp.exp(jnp.sum(jnp.where(after[:, :, None], lasts[None, :, :], 0.0), axis=1))
    t_hi, t_lo = split2(w_all.astype(jnp.float32) * jnp.repeat(tail, HEAD_DIM, axis=1)[:, None, :])
    t_hi = t_hi.reshape(blocks * length, channels)
    t_lo = t_lo.reshape(blocks * length, channels)
    contract = (((0,), (0,)), ((), ()))
    row_state = lax.dot_general(
        t_hi, b_flat, contract, preferred_element_type=jnp.float32
    ) + lax.dot_general(t_lo, b_flat, contract, preferred_element_type=jnp.float32)
    row_decay = jnp.sum(lasts, axis=0)
    extra = jnp.zeros((8, width), jnp.float32).at[0, :heads_here].set(row_decay)
    rows_all = lax.all_gather(jnp.concatenate([row_state, extra], 0), "cy")
    rows = rows_all.shape[0]
    row = lax.axis_index("cy")
    states = rows_all[:, :channels]
    decays = rows_all[:, channels, :heads_here]
    order_rows = jnp.arange(rows)
    between_rows = (order_rows[:, None] < order_rows[None, :]) & (order_rows[None, :] < row)
    span_rows = jnp.sum(jnp.where(between_rows[:, :, None], decays[None, :, :], 0.0), axis=1)
    gain_rows = jnp.where((order_rows < row)[:, None], jnp.exp(span_rows), 0.0)
    entering = jnp.sum(states * jnp.repeat(gain_rows, HEAD_DIM, axis=1)[:, :, None], axis=0)
    before = jnp.sum(jnp.where((order < mine)[:, None], lasts, 0.0), axis=0)
    entering = entering * jnp.repeat(jnp.exp(before), HEAD_DIM)[:, None]
    e_hi, e_lo = split2(entering)
    contract_state = (((1,), (1,)), ((), ()))
    carried = carried + lax.dot_general(
        c_flat, e_hi, contract_state, preferred_element_type=jnp.float32
    ) + lax.dot_general(c_flat, e_lo, contract_state, preferred_element_type=jnp.float32)
    carried = carried.reshape(length, heads_here, HEAD_DIM)
    carried = carried * jnp.exp(cumulative)[:, :, None]
    ssm_out = inner_out + carried + d_skip[None, :, None] * xconv.astype(jnp.float32)
    gated = ssm_out.reshape(length, channels) * jax.nn.silu(z_in.astype(jnp.float32))
    norm_size = per_group * HEAD_DIM
    owners = lax.psum(1, "tp")
    span_tp = per_group // heads_here
    partial_squares = jnp.sum(gated * gated, axis=-1)
    unscaled = (gated * norm_gain[None, :]).astype(jnp.bfloat16)
    partial_out = jnp.dot(unscaled, w_out, preferred_element_type=jnp.float32)
    pieces_out = partial_out.astype(jnp.bfloat16).reshape(length, owners, -1).transpose(1, 0, 2)
    cols = pieces_out.shape[2]
    sq_row = jnp.zeros((cols,), jnp.bfloat16).at[: 3 * length].set(
        jnp.concatenate(split3(partial_squares))
    )
    send = jnp.concatenate(
        [pieces_out, jnp.broadcast_to(sq_row[None, None], (owners, 1, cols))], axis=1
    )
    received = lax.all_to_all(send, "tp", 0, 0, tiled=True)
    parts = received[:, :length].astype(jnp.float32)
    sq = received[:, length, : 3 * length].astype(jnp.float32)
    src_squares = sq[:, :length] + sq[:, length : 2 * length] + sq[:, 2 * length :]
    group_squares = jnp.sum(src_squares.reshape(owners // span_tp, span_tp, length), axis=1)
    scale = lax.rsqrt(group_squares / norm_size + 1e-05)
    scale_src = jnp.repeat(scale, span_tp, axis=0)
    summed = jnp.sum(parts * scale_src[:, :, None], axis=0).astype(jnp.bfloat16)
    return summed


def solution(mesh):
    grid = mesh.devices
    inner = 8 if grid.shape[0] % 8 == 0 else 1
    split = jax.sharding.Mesh(
        grid.reshape(grid.shape[0] // inner, inner, grid.shape[1]), ("cy", "cz", "tp")
    )
    ctx = ("cy", "cz")
    return jax.shard_map(
        local,
        mesh=split,
        in_specs=(
            P(ctx, "tp"),
            P(ctx, "tp"),
            P(ctx, None, None),
            P(ctx, None, None),
            P(None, "tp"),
            P(),
            P(ctx, "tp"),
            P("tp"),
            P("tp"),
            P("tp"),
            P("tp"),
            P("tp", None),
        ),
        out_specs=P(ctx, "tp"),
        check_vma=False,
    )
```
